256 devices in a mesh: dp: 4 (over x), expert: 64 (over y, z, core).
Axes of the slice: x: 4, y: 4, z: 8, core: 2. Of those that a mesh axis runs over, the one named last changes fastest.
Arguments:
- features: bfloat16 [65536, 512], P(('dp', 'expert')), may hold values from -6 to 6
- slots: int32 [65536], P(('dp', 'expert')), may hold values from 0 to 31
- routes: int32 [65536, 2], P(('dp', 'expert')), may hold values from 0 to 63, all different within a row; in each aligned block of 256 rows (0 to 255, 256 to 511, ...) at most 16 rows name the same one
- cotangent: bfloat16 [65536, 512], P(('dp', 'expert')), may hold values from -1.5 to 1.5
- pos_table: bfloat16 [32, 64], replicated, may hold values from -6 to 6
- tower_in: bfloat16 [64, 256], replicated, may hold values from -0.75 to 0.75
- tower_out: bfloat16 [256, 512], replicated, may hold values from -0.375 to 0.375
- router: bfloat16 [512, 64], replicated, may hold values from -0.5 to 0.5
- w_up: bfloat16 [64, 512, 2048], P('expert'), may hold values from -0.25 to 0.25
- w_down: bfloat16 [64, 2048, 512], P('expert'), may hold values from -0.125 to 0.125
Outputs:
- layer_out: bfloat16 [65536, 512], P(('dp', 'expert'))
- grad_in: bfloat16 [65536, 512], P(('dp', 'expert'))
- grad_up: bfloat16 [64, 512, 2048], P('expert')
- grad_down: bfloat16 [64, 2048, 512], P('expert')
The draws below stay inside these ranges and needn't reach their ends.
Inputs may be any that keep to these rules, and one draw needn't show every extreme that they name: `routes`: within the rows of one device no expert is named by more than 16 rows; in some devices' rows one expert is named by exactly 16.
All inputs are finite; a program needn't handle non-finite values.
Results may differ from the reference program's by a relative error of at most 0.013.
Values may be sent and summed in bfloat16 or wider, within the bound.
No kernel may reach another device: no remote copies, remote signals or barrier semaphores. Data moves between devices by JAX's collectives and lax.ppermute only.
A program may use at most 128 MiB of HBM per device.

```python
import math
import jax
import jax.numpy as jnp
import numpy as np
from jax import lax

D = 512
H = 2048
PE = 64
TW = 256
SLOTS = 32
TOP = 2
TOK_DEV = 256
EXPERTS = 64
CAP = 16
TOKENS = 65536
N_DP = 4
N_EXPERT = 64


def place_ends(values, key, least, high):
    dims = values.shape
    index_at = [jax.random.randint(jax.random.fold_in(key, axis), (), 0, dims[axis]) for axis in range(len(dims))]
    values = values.at[tuple(index_at)].set(least)
    longest = dims.index(max(dims))
    index_at[longest] = (index_at[longest] + 1) % dims[longest]
    return values.at[tuple(index_at)].set(high)


def block_scale(own_key, shape, pieces, least, high):
    gain, own = 1.0, jax.random.fold_in(own_key, 6)
    for dim, blocks in pieces:
        heights = jnp.exp(jax.random.uniform(jax.random.fold_in(own, dim), (blocks,), jnp.float32, least / len(pieces), high / len(pieces)))
        gain = gain * jnp.repeat(heights, shape[dim] // blocks).reshape([-1 if axis == dim else 1 for axis in range(len(shape))])
    return gain


def deal_out(rng, own, number, rows, amount, top, limit, slope):
    order = jax.random.permutation(rng, amount)
    crowded, usual = portions_of(amount, rows * top, limit, slope, True), portions_of(amount, rows * top, limit, slope, False)
    places = jnp.arange(amount)

    def named(sizes, turn):
        used = int((sizes > 0).sum())
        fixed = max(1, used // 4)
        passed = fixed + (places - fixed + turn * (used - fixed)) % max(1, amount - fixed)
        return jnp.zeros((amount,), jnp.int32).at[order[jnp.where(places < fixed, places, passed)]].set(jnp.asarray(sizes, jnp.int32))

    sizes = jnp.where(number % 4 == 0, named(crowded, number // 4), named(usual, number - number // 4 - 1))
    mixed = jax.random.permutation(jax.random.fold_in(own, 3), amount)
    giver, sink = mixed[0:amount // 2 * 2:2], mixed[1:amount // 2 * 2:2]
    slack = jnp.minimum(sizes[giver] - 1, limit - sizes[sink]) // 2
    slack = jnp.where((giver == order[0]) | (sink == order[0]) | (sizes[sink] == 0), 0, jnp.maximum(slack, 0))
    passed = jax.random.randint(jax.random.fold_in(own, 4), (amount // 2,), 0, 1 << 20) % (slack + 1)
    sizes = sizes.at[giver].add(-passed).at[sink].add(passed)
    members = jnp.searchsorted(jnp.cumsum(sizes), jnp.arange(rows * top), side="right").astype(jnp.int32)
    table = members.reshape(top, rows).T
    table = table[jax.random.permutation(jax.random.fold_in(own, 1), rows)]
    turn = jax.random.randint(jax.random.fold_in(own, 2), (rows, 1), 0, top)
    return jnp.take_along_axis(table, (jnp.arange(top)[None, :] + turn) % top, axis=1)


def portions_of(amount, total, reach, slope, full):
    weights = [(1 << 20) // math.isqrt(standing ** slope) + 1 for standing in range(1, amount + 1)]
    largest = reach if full else min(reach, max(-(-total // amount), total * weights[0] // sum(weights)))
    least = 1 if total - largest >= amount - 1 else 0
    counts, surplus = [largest] + [least] * (amount - 1), total - largest - least * (amount - 1)
    while surplus > 0:
        free = [i for i in range(1, amount) if counts[i] < largest] or [i for i in range(1, amount) if counts[i] < reach]
        mass, remaining = sum([weights[i] for i in free]), surplus
        for i in free:
            extra = min(reach - counts[i], max(1, remaining * weights[i] // mass), surplus)
            counts[i] = counts[i] + extra
            surplus = surplus - extra
    return np.array(counts)


def normal_values(stream_key, shape, deviation, reach, cuts=(), kind=jnp.bfloat16):
    entries = deviation * jax.random.normal(stream_key, shape, jnp.float32)
    if cuts:
        entries = entries * block_scale(stream_key, shape, cuts, -0.22, 0.18)
    return jnp.clip(entries, -reach, reach).astype(kind)


def setup_inputs(seed: int = 0) -> dict:
    splits = jax.random.split(jax.random.key(seed), 11)
    features = normal_values(splits[0], (TOKENS, D), 1.0, 6.0, ((0, 256),))
    slots = place_ends(jax.random.randint(splits[1], (TOKENS,), 0, SLOTS), jax.random.fold_in(splits[1], 1), 0, SLOTS - 1).astype(jnp.int32)
    routes_keys = jax.random.split(jax.random.fold_in(splits[2], 1), TOKENS // TOK_DEV)
    routes_turns = jax.random.permutation(jax.random.fold_in(splits[2], 3), TOKENS // TOK_DEV)
    routes = jax.vmap(lambda own, number: deal_out(jax.random.fold_in(splits[2], 2), own, number, TOK_DEV, EXPERTS, TOP, CAP, 2))(routes_keys, routes_turns).reshape((TOKENS, TOP))
    cotangent = normal_values(splits[3], (TOKENS, D), 0.25, 1.5, ((0, 256),))
    pos_table = normal_values(splits[4], (SLOTS, PE), 1.0, 6.0)
    tower_in = normal_values(splits[5], (PE, TW), PE ** -0.5, 0.75)
    tower_out = normal_values(splits[6], (TW, D), TW ** -0.5, 0.375)
    router = normal_values(splits[7], (D, EXPERTS), (D // 4) ** -0.5, 0.5)
    w_up = normal_values(splits[8], (EXPERTS, D, H), D ** -0.5, 0.25, ((0, 64),))
    w_down = normal_values(splits[9], (EXPERTS, H, D), H ** -0.5, 0.125, ((0, 64),))
    return {"features": features, "slots": slots, "routes": routes, "cotangent": cotangent, "pos_table": pos_table, "tower_in": tower_in, "tower_out": tower_out, "router": router, "w_up": w_up, "w_down": w_down}


coef_a = 0.7978845608028654
coef_b = 0.044715


def gelu_pair(pre_act):
    inner = coef_a * (pre_act + coef_b * pre_act * pre_act * pre_act)
    tanh_val = jnp.tanh(inner)
    activated = 0.5 * pre_act * (1.0 + tanh_val)
    gelu_slope = 0.5 * (1.0 + tanh_val) + 0.5 * pre_act * (1.0 - tanh_val * tanh_val) * coef_a * (1.0 + 3.0 * coef_b * pre_act * pre_act)
    return activated, gelu_slope


def expert_pass(packed):
    inputs_rows, cot_rows, w_up_one, w_down_one = packed
    pre_act = jnp.dot(inputs_rows, w_up_one, preferred_element_type=jnp.float32)
    activated, gelu_slope = gelu_pair(pre_act)
    hidden = activated.astype(jnp.bfloat16)
    outputs = jnp.dot(hidden, w_down_one, preferred_element_type=jnp.float32).astype(jnp.bfloat16)
    d_hidden = jnp.dot(cot_rows, w_down_one.T, preferred_element_type=jnp.float32)
    d_pre = (d_hidden * gelu_slope).astype(jnp.bfloat16)
    grad_down_part = jnp.dot(hidden.T, cot_rows, preferred_element_type=jnp.float32).astype(jnp.bfloat16)
    grad_up_part = jnp.dot(inputs_rows.T, d_pre, preferred_element_type=jnp.float32).astype(jnp.bfloat16)
    d_inputs = jnp.dot(d_pre, w_up_one.T, preferred_element_type=jnp.float32).astype(jnp.bfloat16)
    return outputs, d_inputs, grad_up_part, grad_down_part


def reference(features, slots, routes, cotangent, pos_table, tower_in, tower_out, router, w_up, w_down):
    pos_hidden = jax.nn.relu(jnp.dot(pos_table, tower_in, preferred_element_type=jnp.float32))
    pos_rows = jnp.dot(pos_hidden, tower_out.astype(jnp.float32), precision=lax.Precision.HIGHEST)
    mixed_in = (features.astype(jnp.float32) + pos_rows[slots]).astype(jnp.bfloat16)
    logits = jnp.dot(mixed_in, router, preferred_element_type=jnp.float32)
    chosen = jnp.take_along_axis(logits, routes, axis=1)
    squashed = 1.0 / (1.0 + jnp.exp(-chosen))
    gate_total = jnp.sum(squashed, axis=1, keepdims=True)
    gates = squashed / gate_total
    cot_wide = cotangent.astype(jnp.float32)
    slot_cot = (gates[:, :, None] * cot_wide[:, None, :]).astype(jnp.bfloat16)
    group_rows = N_EXPERT * TOK_DEV
    span = N_EXPERT * CAP
    expert_ids = jnp.arange(EXPERTS, dtype=jnp.int32)
    out_blocks = []
    grad_blocks = []
    up_total = jnp.zeros((EXPERTS, D, H), jnp.float32)
    down_total = jnp.zeros((EXPERTS, H, D), jnp.float32)
    for group_index in range(N_DP):
        first_row = group_index * group_rows
        block_routes = routes[first_row:first_row + group_rows].reshape(-1)
        block_hot = (block_routes[:, None] == expert_ids[None, :]).astype(jnp.int32)
        before = jnp.cumsum(block_hot, axis=0, dtype=jnp.int32) - block_hot
        slot_rank = jnp.sum(before * block_hot, axis=1, dtype=jnp.int32).astype(jnp.int32)
        slot_place = (block_routes * span + slot_rank).astype(jnp.int32)
        rows_in = jnp.repeat(mixed_in[first_row:first_row + group_rows], TOP, axis=0)
        rows_cot = slot_cot[first_row:first_row + group_rows].reshape(-1, D)
        buffer_in = jnp.zeros((EXPERTS * span, D), jnp.bfloat16).at[slot_place].set(rows_in).reshape(EXPERTS, span, D)
        buffer_cot = jnp.zeros((EXPERTS * span, D), jnp.bfloat16).at[slot_place].set(rows_cot).reshape(EXPERTS, span, D)
        outputs, d_inputs, grad_up_part, grad_down_part = lax.map(expert_pass, (buffer_in, buffer_cot, w_up, w_down))
        grad_up_part = lax.optimization_barrier(grad_up_part)
        grad_down_part = lax.optimization_barrier(grad_down_part)
        up_total = up_total + grad_up_part.astype(jnp.float32)
        down_total = down_total + grad_down_part.astype(jnp.float32)
        out_blocks.append(outputs.reshape(-1, D)[slot_place].reshape(group_rows, TOP, D))
        grad_blocks.append(d_inputs.reshape(-1, D)[slot_place].reshape(group_rows, TOP, D))
    expert_out = jnp.concatenate(out_blocks, axis=0)
    slot_grad = jnp.concatenate(grad_blocks, axis=0)
    layer_out = (mixed_in.astype(jnp.float32) + jnp.sum(gates[:, :, None] * expert_out.astype(jnp.float32), axis=1)).astype(jnp.bfloat16)
    d_gates = jnp.sum(expert_out.astype(jnp.float32) * cot_wide[:, None, :], axis=2)
    mean_term = jnp.sum(gates * d_gates, axis=1, keepdims=True)
    d_chosen = (d_gates - mean_term) / gate_total * squashed * (1.0 - squashed)
    route_hot = routes[:, :, None] == expert_ids[None, None, :]
    d_logits = jnp.sum(jnp.where(route_hot, d_chosen[:, :, None], 0.0), axis=1)
    d_router = jnp.dot(d_logits, router.astype(jnp.float32).T, precision=lax.Precision.HIGHEST)
    grad_in = (cot_wide + jnp.sum(slot_grad.astype(jnp.float32), axis=1) + d_router).astype(jnp.bfloat16)
    return layer_out, grad_in, up_total.astype(jnp.bfloat16), down_total.astype(jnp.bfloat16)
```

```python
import jax
import jax.numpy as jnp
from jax import lax
from jax.sharding import PartitionSpec as P

TOP = 2


coef_a = 0.7978845608028654
coef_b = 0.044715


def gelu_pair(pre_act):
    inner = coef_a * (pre_act + coef_b * pre_act * pre_act * pre_act)
    tanh_val = jnp.tanh(inner)
    activated = 0.5 * pre_act * (1.0 + tanh_val)
    gelu_slope = 0.5 * (1.0 + tanh_val) + 0.5 * pre_act * (1.0 - tanh_val * tanh_val) * coef_a * (
        1.0 + 3.0 * coef_b * pre_act * pre_act
    )
    return (activated, gelu_slope)


def contract_rows(left, right):
    return lax.dot_general(
        left, right, (((0,), (0,)), ((), ())), preferred_element_type=jnp.float32
    )


def contract_cols(left, right):
    return lax.dot_general(
        left, right, (((1,), (1,)), ((), ())), preferred_element_type=jnp.float32
    )


def expert_forward(flat_in, w_up_one, w_down_one):
    pre_act = jnp.dot(flat_in, w_up_one, preferred_element_type=jnp.float32)
    activated, gelu_slope = gelu_pair(pre_act)
    hidden = activated.astype(jnp.bfloat16)
    outputs = jnp.dot(hidden, w_down_one, preferred_element_type=jnp.float32).astype(jnp.bfloat16)
    return (hidden, gelu_slope, outputs)


def expert_backward(flat_in, flat_cot, hidden, gelu_slope, w_up_one, w_down_one):
    grad_down_part = contract_rows(hidden, flat_cot)
    d_hidden = contract_cols(flat_cot, w_down_one)
    d_pre = (d_hidden * gelu_slope).astype(jnp.bfloat16)
    d_inputs = contract_cols(d_pre, w_up_one).astype(jnp.bfloat16)
    grad_up_part = contract_rows(flat_in, d_pre)
    sum_up, sum_down = (
        lax.psum(grad_up_part.astype(jnp.bfloat16), "dp").astype(jnp.float32),
        lax.psum(grad_down_part.astype(jnp.bfloat16), "dp").astype(jnp.float32),
    )
    return (d_inputs, sum_up, sum_down)


def per_device(
    features, slots, routes, cotangent, pos_table, tower_in, tower_out, router, w_up, w_down
):
    tok_rows = features.shape[0]
    feature_width = features.shape[1]
    n_experts = router.shape[1]
    capacity = 2 * TOP * tok_rows // n_experts
    pos_hidden = jax.nn.relu(jnp.dot(pos_table, tower_in, preferred_element_type=jnp.float32))
    pos_rows = jnp.dot(pos_hidden, tower_out.astype(jnp.float32), precision=lax.Precision.HIGHEST)
    slot_hot = (slots[:, None] == jnp.arange(pos_table.shape[0], dtype=jnp.int32)[None, :]).astype(
        jnp.float32
    )
    pos_feats = jnp.dot(slot_hot, pos_rows, precision=lax.Precision.HIGHEST)
    mixed_in = (features.astype(jnp.float32) + pos_feats).astype(jnp.bfloat16)
    logits = jnp.dot(mixed_in, router, preferred_element_type=jnp.float32)
    expert_ids = jnp.arange(n_experts, dtype=jnp.int32)
    route_hot = routes[:, :, None] == expert_ids[None, None, :]
    chosen = jnp.sum(jnp.where(route_hot, logits[:, None, :], 0.0), axis=2)
    squashed = 1.0 / (1.0 + jnp.exp(-chosen))
    gate_total = jnp.sum(squashed, axis=1, keepdims=True)
    gates = squashed / gate_total
    cot_wide = cotangent.astype(jnp.float32)
    slot_cot = (gates[:, :, None] * cot_wide[:, None, :]).astype(jnp.bfloat16)
    flat_routes = routes.reshape(-1)
    flat_hot = route_hot.reshape(-1, n_experts).astype(jnp.int32)
    before = jnp.cumsum(flat_hot, axis=0, dtype=jnp.int32) - flat_hot
    slot_rank = jnp.sum(before * flat_hot, axis=1, dtype=jnp.int32)
    slot_place = flat_routes * capacity + slot_rank
    pair_shape = (n_experts, 2 * capacity, feature_width)
    cot_place = slot_place + flat_routes * capacity + capacity
    in_place = slot_place + flat_routes * capacity
    send_rows = jnp.concatenate([jnp.repeat(mixed_in, TOP, axis=0), slot_cot.reshape(-1, feature_width)])
    send_pair = (
        jnp.zeros((n_experts * 2 * capacity, feature_width), jnp.bfloat16)
        .at[jnp.concatenate([in_place, cot_place])]
        .set(send_rows)
        .reshape(pair_shape)
    )
    w_up_one = w_up[0]
    w_down_one = w_down[0]
    recv_pair = lax.all_to_all(send_pair, "expert", split_axis=0, concat_axis=0, tiled=True)
    flat_in = recv_pair[:, :capacity].reshape(-1, feature_width)
    flat_cot = recv_pair[:, capacity:].reshape(-1, feature_width)
    hidden, gelu_slope, outputs = expert_forward(flat_in, w_up_one, w_down_one)
    d_inputs, sum_up, sum_down = expert_backward(
        flat_in, flat_cot, hidden, gelu_slope, w_up_one, w_down_one
    )
    back_pair = jnp.concatenate(
        [outputs.reshape(n_experts, capacity, feature_width), d_inputs.reshape(n_experts, capacity, feature_width)],
        axis=1,
    )
    back_pair = lax.all_to_all(back_pair, "expert", split_axis=0, concat_axis=0, tiled=True)
    back_flat = back_pair.reshape(-1, feature_width)
    expert_out = back_flat[in_place].reshape(tok_rows, TOP, feature_width)
    slot_grad = back_flat[cot_place].reshape(tok_rows, TOP, feature_width)
    expert_wide = expert_out.astype(jnp.float32)
    layer_out = (
        mixed_in.astype(jnp.float32) + jnp.sum(gates[:, :, None] * expert_wide, axis=1)
    ).astype(jnp.bfloat16)
    d_gates = jnp.sum(expert_wide * cot_wide[:, None, :], axis=2)
    mean_term = jnp.sum(gates * d_gates, axis=1, keepdims=True)
    d_chosen = (d_gates - mean_term) / gate_total * squashed * (1.0 - squashed)
    d_logits = jnp.sum(jnp.where(route_hot, d_chosen[:, :, None], 0.0), axis=1)
    d_router = lax.dot_general(
        d_logits,
        router.astype(jnp.float32),
        (((1,), (1,)), ((), ())),
        precision=lax.Precision.HIGHEST,
    )
    grad_in = (cot_wide + jnp.sum(slot_grad.astype(jnp.float32), axis=1) + d_router).astype(
        jnp.bfloat16
    )
    return (
        layer_out,
        grad_in,
        sum_up.astype(jnp.bfloat16)[None],
        sum_down.astype(jnp.bfloat16)[None],
    )


def solution(mesh):
    return jax.shard_map(
        per_device,
        mesh=mesh,
        in_specs=(
            P(("dp", "expert"), None),
            P(("dp", "expert")),
            P(("dp", "expert"), None),
            P(("dp", "expert"), None),
            P(),
            P(),
            P(),
            P(),
            P("expert", None, None),
            P("expert", None, None),
        ),
        out_specs=(
            P(("dp", "expert"), None),
            P(("dp", "expert"), None),
            P("expert", None, None),
            P("expert", None, None),
        ),
        check_vma=False,
    )
```

```python
import jax
import jax.numpy as jnp
from jax import lax
from jax.sharding import PartitionSpec as P

TOP = 2


coef_a = 0.7978845608028654
coef_b = 0.044715


def gelu_pair(pre_act):
    inner = coef_a * (pre_act + coef_b * pre_act * pre_act * pre_act)
    tanh_val = jnp.tanh(inner)
    activated = 0.5 * pre_act * (1.0 + tanh_val)
    gelu_slope = 0.5 * (1.0 + tanh_val) + 0.5 * pre_act * (1.0 - tanh_val * tanh_val) * coef_a * (
        1.0 + 3.0 * coef_b * pre_act * pre_act
    )
    return (activated, gelu_slope)


def contract_rows(left, right):
    return lax.dot_general(
        left, right, (((0,), (0,)), ((), ())), preferred_element_type=jnp.float32
    )


def contract_cols(left, right):
    return lax.dot_general(
        left, right, (((1,), (1,)), ((), ())), preferred_element_type=jnp.float32
    )


def expert_forward(flat_in, w_up_one, w_down_one):
    pre_act = jnp.dot(flat_in, w_up_one, preferred_element_type=jnp.float32)
    activated, gelu_slope = gelu_pair(pre_act)
    hidden = activated.astype(jnp.bfloat16)
    outputs = jnp.dot(hidden, w_down_one, preferred_element_type=jnp.float32).astype(jnp.bfloat16)
    return (hidden, gelu_slope, outputs)


def expert_backward(flat_in, flat_cot, hidden, gelu_slope, w_up_one, w_down_one):
    grad_down_part = contract_rows(hidden, flat_cot)
    d_hidden = contract_cols(flat_cot, w_down_one)
    d_pre = (d_hidden * gelu_slope).astype(jnp.bfloat16)
    d_inputs = contract_cols(d_pre, w_up_one).astype(jnp.bfloat16)
    grad_up_part = contract_rows(flat_in, d_pre)
    return (d_inputs, grad_up_part, grad_down_part)


def per_device(
    features, slots, routes, cotangent, pos_table, tower_in, tower_out, router, w_up, w_down
):
    tok_rows = features.shape[0]
    feature_width = features.shape[1]
    n_experts = router.shape[1]
    capacity = 2 * TOP * tok_rows // n_experts
    pos_hidden = jax.nn.relu(jnp.dot(pos_table, tower_in, preferred_element_type=jnp.float32))
    pos_rows = jnp.dot(pos_hidden, tower_out.astype(jnp.float32), precision=lax.Precision.HIGHEST)
    slot_hot = (slots[:, None] == jnp.arange(pos_table.shape[0], dtype=jnp.int32)[None, :]).astype(
        jnp.float32
    )
    pos_feats = jnp.dot(slot_hot, pos_rows, precision=lax.Precision.HIGHEST)
    mixed_in = (features.astype(jnp.float32) + pos_feats).astype(jnp.bfloat16)
    logits = jnp.dot(mixed_in, router, preferred_element_type=jnp.float32)
    expert_ids = jnp.arange(n_experts, dtype=jnp.int32)
    route_hot = routes[:, :, None] == expert_ids[None, None, :]
    chosen = jnp.sum(jnp.where(route_hot, logits[:, None, :], 0.0), axis=2)
    squashed = 1.0 / (1.0 + jnp.exp(-chosen))
    gate_total = jnp.sum(squashed, axis=1, keepdims=True)
    gates = squashed / gate_total
    cot_wide = cotangent.astype(jnp.float32)
    slot_cot = (gates[:, :, None] * cot_wide[:, None, :]).astype(jnp.bfloat16)
    flat_routes = routes.reshape(-1)
    flat_hot = route_hot.reshape(-1, n_experts).astype(jnp.int32)
    before = jnp.cumsum(flat_hot, axis=0, dtype=jnp.int32) - flat_hot
    slot_rank = jnp.sum(before * flat_hot, axis=1, dtype=jnp.int32)
    slot_place = flat_routes * capacity + slot_rank
    half = capacity // 2
    chunk_shape = (n_experts, 2 * half, feature_width)
    in_place = flat_routes * (2 * capacity) + (slot_rank // half) * (2 * half) + slot_rank % half
    cot_place = in_place + half
    send_rows = jnp.concatenate([jnp.repeat(mixed_in, TOP, axis=0), slot_cot.reshape(-1, feature_width)])
    send_pair = (
        jnp.zeros((n_experts * 2 * capacity, feature_width), jnp.bfloat16)
        .at[jnp.concatenate([in_place, cot_place])]
        .set(send_rows)
        .reshape(n_experts, 2 * capacity, feature_width)
    )
    w_up_one = w_up[0]
    w_down_one = w_down[0]
    backs = []
    grad_ups = []
    grad_downs = []
    for chunk in range(2):
        sent = send_pair[:, chunk * 2 * half:(chunk + 1) * 2 * half]
        recv = lax.all_to_all(sent, "expert", split_axis=0, concat_axis=0, tiled=True)
        flat_in = recv[:, :half].reshape(-1, feature_width)
        flat_cot = recv[:, half:].reshape(-1, feature_width)
        hidden, gelu_slope, outputs = expert_forward(flat_in, w_up_one, w_down_one)
        d_inputs, grad_up_part, grad_down_part = expert_backward(
            flat_in, flat_cot, hidden, gelu_slope, w_up_one, w_down_one
        )
        grad_ups.append(grad_up_part)
        grad_downs.append(grad_down_part)
        back = jnp.concatenate(
            [outputs.reshape(n_experts, half, feature_width), d_inputs.reshape(n_experts, half, feature_width)],
            axis=1,
        )
        backs.append(lax.all_to_all(back, "expert", split_axis=0, concat_axis=0, tiled=True))
    sum_up = lax.psum((grad_ups[0] + grad_ups[1]).astype(jnp.bfloat16), "dp")
    sum_down = lax.psum((grad_downs[0] + grad_downs[1]).astype(jnp.bfloat16), "dp")
    back_flat = jnp.concatenate(backs, axis=1).reshape(-1, feature_width)
    expert_out = back_flat[in_place].reshape(tok_rows, TOP, feature_width)
    slot_grad = back_flat[cot_place].reshape(tok_rows, TOP, feature_width)
    expert_wide = expert_out.astype(jnp.float32)
    layer_out = (
        mixed_in.astype(jnp.float32) + jnp.sum(gates[:, :, None] * expert_wide, axis=1)
    ).astype(jnp.bfloat16)
    d_gates = jnp.sum(expert_wide * cot_wide[:, None, :], axis=2)
    mean_term = jnp.sum(gates * d_gates, axis=1, keepdims=True)
    d_chosen = (d_gates - mean_term) / gate_total * squashed * (1.0 - squashed)
    d_logits = jnp.sum(jnp.where(route_hot, d_chosen[:, :, None], 0.0), axis=1)
    d_router = lax.dot_general(
        d_logits,
        router.astype(jnp.float32),
        (((1,), (1,)), ((), ())),
        precision=lax.Precision.HIGHEST,
    )
    grad_in = (cot_wide + jnp.sum(slot_grad.astype(jnp.float32), axis=1) + d_router).astype(
        jnp.bfloat16
    )
    return (
        layer_out,
        grad_in,
        sum_up.astype(jnp.bfloat16)[None],
        sum_down.astype(jnp.bfloat16)[None],
    )


def solution(mesh):
    return jax.shard_map(
        per_device,
        mesh=mesh,
        in_specs=(
            P(("dp", "expert"), None),
            P(("dp", "expert")),
            P(("dp", "expert"), None),
            P(("dp", "expert"), None),
            P(),
            P(),
            P(),
            P(),
            P("expert", None, None),
            P("expert", None, None),
        ),
        out_specs=(
            P(("dp", "expert"), None),
            P(("dp", "expert"), None),
            P("expert", None, None),
            P("expert", None, None),
        ),
        check_vma=False,
    )
```

```python
import jax
import jax.numpy as jnp
from jax import lax
from jax.sharding import PartitionSpec as P

TOP = 2


coef_a = 0.7978845608028654
coef_b = 0.044715


def gelu_pair(pre_act):
    inner = coef_a * (pre_act + coef_b * pre_act * pre_act * pre_act)
    tanh_val = jnp.tanh(inner)
    activated = 0.5 * pre_act * (1.0 + tanh_val)
    gelu_slope = 0.5 * (1.0 + tanh_val) + 0.5 * pre_act * (1.0 - tanh_val * tanh_val) * coef_a * (
        1.0 + 3.0 * coef_b * pre_act * pre_act
    )
    return (activated, gelu_slope)


def contract_rows(left, right):
    return lax.dot_general(
        left, right, (((0,), (0,)), ((), ())), preferred_element_type=jnp.float32
    )


def contract_cols(left, right):
    return lax.dot_general(
        left, right, (((1,), (1,)), ((), ())), preferred_element_type=jnp.float32
    )


def expert_forward(flat_in, w_up_one, w_down_one):
    pre_act = jnp.dot(flat_in, w_up_one, preferred_element_type=jnp.float32)
    activated, gelu_slope = gelu_pair(pre_act)
    hidden = activated.astype(jnp.bfloat16)
    outputs = jnp.dot(hidden, w_down_one, preferred_element_type=jnp.float32).astype(jnp.bfloat16)
    return (hidden, gelu_slope, outputs)


def expert_backward(flat_in, flat_cot, hidden, gelu_slope, w_up_one, w_down_one):
    grad_down_part = contract_rows(hidden, flat_cot)
    d_hidden = contract_cols(flat_cot, w_down_one)
    d_pre = (d_hidden * gelu_slope).astype(jnp.bfloat16)
    d_inputs = contract_cols(d_pre, w_up_one).astype(jnp.bfloat16)
    grad_up_part = contract_rows(flat_in, d_pre)
    return (d_inputs, grad_up_part, grad_down_part)


def dp_allreduce(parts, axis, n):
    me = lax.axis_index(axis)
    rings = ([(j, (j + 1) % n) for j in range(n)], [(j, (j - 1) % n) for j in range(n)])
    acc = [
        [p.reshape(2, n, p.shape[0] // (2 * n), p.shape[1])[d].astype(jnp.float32) for p in parts]
        for d in range(2)
    ]
    for step in range(n - 1):
        for d in range(2):
            sign = 1 - 2 * d
            send_at = (me - sign * step) % n
            recv_at = (me - sign * (step + 1)) % n
            sent = [lax.dynamic_index_in_dim(a, send_at, 0, False).astype(jnp.bfloat16) for a in acc[d]]
            got = lax.ppermute(sent, axis, rings[d])
            acc[d] = [
                lax.dynamic_update_index_in_dim(
                    a, lax.dynamic_index_in_dim(a, recv_at, 0, False) + g.astype(jnp.float32), recv_at, 0
                )
                for a, g in zip(acc[d], got)
            ]
    held = [[a.astype(jnp.bfloat16) for a in acc[d]] for d in range(2)]
    for step in range(n - 1):
        for d in range(2):
            sign = 1 - 2 * d
            send_at = (me + sign * (1 - step)) % n
            recv_at = (me - sign * step) % n
            sent = [lax.dynamic_index_in_dim(a, send_at, 0, False) for a in held[d]]
            got = lax.ppermute(sent, axis, rings[d])
            held[d] = [lax.dynamic_update_index_in_dim(a, g, recv_at, 0) for a, g in zip(held[d], got)]
    return [
        jnp.stack([held[0][k], held[1][k]]).reshape(p.shape) for k, p in enumerate(parts)
    ]


def per_device(
    features, slots, routes, cotangent, pos_table, tower_in, tower_out, router, w_up, w_down
):
    tok_rows = features.shape[0]
    feature_width = features.shape[1]
    n_experts = router.shape[1]
    capacity = 2 * TOP * tok_rows // n_experts
    pos_hidden = jax.nn.relu(jnp.dot(pos_table, tower_in, preferred_element_type=jnp.float32))
    pos_rows = jnp.dot(pos_hidden, tower_out.astype(jnp.float32), precision=lax.Precision.HIGHEST)
    slot_hot = (slots[:, None] == jnp.arange(pos_table.shape[0], dtype=jnp.int32)[None, :]).astype(
        jnp.float32
    )
    pos_feats = jnp.dot(slot_hot, pos_rows, precision=lax.Precision.HIGHEST)
    mixed_in = (features.astype(jnp.float32) + pos_feats).astype(jnp.bfloat16)
    logits = jnp.dot(mixed_in, router, preferred_element_type=jnp.float32)
    expert_ids = jnp.arange(n_experts, dtype=jnp.int32)
    route_hot = routes[:, :, None] == expert_ids[None, None, :]
    chosen = jnp.sum(jnp.where(route_hot, logits[:, None, :], 0.0), axis=2)
    squashed = 1.0 / (1.0 + jnp.exp(-chosen))
    gate_total = jnp.sum(squashed, axis=1, keepdims=True)
    gates = squashed / gate_total
    cot_wide = cotangent.astype(jnp.float32)
    slot_cot = (gates[:, :, None] * cot_wide[:, None, :]).astype(jnp.bfloat16)
    flat_routes = routes.reshape(-1)
    flat_hot = route_hot.reshape(-1, n_experts).astype(jnp.int32)
    before = jnp.cumsum(flat_hot, axis=0, dtype=jnp.int32) - flat_hot
    slot_rank = jnp.sum(before * flat_hot, axis=1, dtype=jnp.int32)
    slot_place = flat_routes * capacity + slot_rank
    half = capacity // 2
    chunk_shape = (n_experts, 2 * half, feature_width)
    in_place = flat_routes * (2 * capacity) + (slot_rank // half) * (2 * half) + slot_rank % half
    cot_place = in_place + half
    send_rows = jnp.concatenate([jnp.repeat(mixed_in, TOP, axis=0), slot_cot.reshape(-1, feature_width)])
    send_pair = (
        jnp.zeros((n_experts * 2 * capacity, feature_width), jnp.bfloat16)
        .at[jnp.concatenate([in_place, cot_place])]
        .set(send_rows)
        .reshape(n_experts, 2 * capacity, feature_width)
    )
    w_up_one = w_up[0]
    w_down_one = w_down[0]
    backs = []
    grad_ups = []
    grad_downs = []
    for chunk in range(2):
        sent = send_pair[:, chunk * 2 * half:(chunk + 1) * 2 * half]
        recv = lax.all_to_all(sent, "expert", split_axis=0, concat_axis=0, tiled=True)
        flat_in = recv[:, :half].reshape(-1, feature_width)
        flat_cot = recv[:, half:].reshape(-1, feature_width)
        hidden, gelu_slope, outputs = expert_forward(flat_in, w_up_one, w_down_one)
        d_inputs, grad_up_part, grad_down_part = expert_backward(
            flat_in, flat_cot, hidden, gelu_slope, w_up_one, w_down_one
        )
        grad_ups.append(grad_up_part)
        grad_downs.append(grad_down_part)
        back = jnp.concatenate(
            [outputs.reshape(n_experts, half, feature_width), d_inputs.reshape(n_experts, half, feature_width)],
            axis=1,
        )
        backs.append(lax.all_to_all(back, "expert", split_axis=0, concat_axis=0, tiled=True))
    sum_up, sum_down = dp_allreduce(
        [(grad_ups[0] + grad_ups[1]).astype(jnp.bfloat16), (grad_downs[0] + grad_downs[1]).astype(jnp.bfloat16)],
        "dp",
        lax.axis_size("dp"),
    )
    back_flat = jnp.concatenate(backs, axis=1).reshape(-1, feature_width)
    expert_out = back_flat[in_place].reshape(tok_rows, TOP, feature_width)
    slot_grad = back_flat[cot_place].reshape(tok_rows, TOP, feature_width)
    expert_wide = expert_out.astype(jnp.float32)
    layer_out = (
        mixed_in.astype(jnp.float32) + jnp.sum(gates[:, :, None] * expert_wide, axis=1)
    ).astype(jnp.bfloat16)
    d_gates = jnp.sum(expert_wide * cot_wide[:, None, :], axis=2)
    mean_term = jnp.sum(gates * d_gates, axis=1, keepdims=True)
    d_chosen = (d_gates - mean_term) / gate_total * squashed * (1.0 - squashed)
    d_logits = jnp.sum(jnp.where(route_hot, d_chosen[:, :, None], 0.0), axis=1)
    d_router = lax.dot_general(
        d_logits,
        router.astype(jnp.float32),
        (((1,), (1,)), ((), ())),
        precision=lax.Precision.HIGHEST,
    )
    grad_in = (cot_wide + jnp.sum(slot_grad.astype(jnp.float32), axis=1) + d_router).astype(
        jnp.bfloat16
    )
    return (
        layer_out,
        grad_in,
        sum_up.astype(jnp.bfloat16)[None],
        sum_down.astype(jnp.bfloat16)[None],
    )


def solution(mesh):
    return jax.shard_map(
        per_device,
        mesh=mesh,
        in_specs=(
            P(("dp", "expert"), None),
            P(("dp", "expert")),
            P(("dp", "expert"), None),
            P(("dp", "expert"), None),
            P(),
            P(),
            P(),
            P(),
            P("expert", None, None),
            P("expert", None, None),
        ),
        out_specs=(
            P(("dp", "expert"), None),
            P(("dp", "expert"), None),
            P("expert", None, None),
            P("expert", None, None),
        ),
        check_vma=False,
    )
```

```python
import jax
import jax.numpy as jnp
from jax import lax
from jax.sharding import PartitionSpec as P

TOP = 2


coef_a = 0.7978845608028654
coef_b = 0.044715


def gelu_pair(pre_act):
    inner = coef_a * (pre_act + coef_b * pre_act * pre_act * pre_act)
    tanh_val = jnp.tanh(inner)
    activated = 0.5 * pre_act * (1.0 + tanh_val)
    gelu_slope = 0.5 * (1.0 + tanh_val) + 0.5 * pre_act * (1.0 - tanh_val * tanh_val) * coef_a * (
        1.0 + 3.0 * coef_b * pre_act * pre_act
    )
    return (activated, gelu_slope)


def contract_rows(left, right):
    return lax.dot_general(
        left, right, (((0,), (0,)), ((), ())), preferred_element_type=jnp.float32
    )


def contract_cols(left, right):
    return lax.dot_general(
        left, right, (((1,), (1,)), ((), ())), preferred_element_type=jnp.float32
    )


def expert_forward(flat_in, w_up_one, w_down_one):
    pre_act = jnp.dot(flat_in, w_up_one, preferred_element_type=jnp.float32)
    activated, gelu_slope = gelu_pair(pre_act)
    hidden = activated.astype(jnp.bfloat16)
    outputs = jnp.dot(hidden, w_down_one, preferred_element_type=jnp.float32).astype(jnp.bfloat16)
    return (hidden, gelu_slope, outputs)


def expert_backward(flat_in, flat_cot, hidden, gelu_slope, w_up_one, w_down_one):
    grad_down_part = contract_rows(hidden, flat_cot)
    d_hidden = contract_cols(flat_cot, w_down_one)
    d_pre = (d_hidden * gelu_slope).astype(jnp.bfloat16)
    d_inputs = contract_cols(d_pre, w_up_one).astype(jnp.bfloat16)
    grad_up_part = contract_rows(flat_in, d_pre)
    return (d_inputs, grad_up_part, grad_down_part)


def per_device(
    features, slots, routes, cotangent, pos_table, tower_in, tower_out, router, w_up, w_down
):
    tok_rows = features.shape[0]
    feature_width = features.shape[1]
    n_experts = router.shape[1]
    capacity = 2 * TOP * tok_rows // n_experts
    pos_hidden = jax.nn.relu(jnp.dot(pos_table, tower_in, preferred_element_type=jnp.float32))
    pos_rows = jnp.dot(pos_hidden, tower_out.astype(jnp.float32), precision=lax.Precision.HIGHEST)
    slot_hot = (slots[:, None] == jnp.arange(pos_table.shape[0], dtype=jnp.int32)[None, :]).astype(
        jnp.float32
    )
    pos_feats = jnp.dot(slot_hot, pos_rows, precision=lax.Precision.HIGHEST)
    mixed_in = (features.astype(jnp.float32) + pos_feats).astype(jnp.bfloat16)
    logits = jnp.dot(mixed_in, router, preferred_element_type=jnp.float32)
    expert_ids = jnp.arange(n_experts, dtype=jnp.int32)
    route_hot = routes[:, :, None] == expert_ids[None, None, :]
    chosen = jnp.sum(jnp.where(route_hot, logits[:, None, :], 0.0), axis=2)
    squashed = 1.0 / (1.0 + jnp.exp(-chosen))
    gate_total = jnp.sum(squashed, axis=1, keepdims=True)
    gates = squashed / gate_total
    cot_wide = cotangent.astype(jnp.float32)
    slot_cot = jnp.concatenate(
        [(gates[:, k:k + 1] * cot_wide).astype(jnp.bfloat16) for k in range(TOP)]
    )
    flat_routes = routes.reshape(-1)
    flat_hot = route_hot.reshape(-1, n_experts).astype(jnp.int32)
    before = jnp.cumsum(flat_hot, axis=0, dtype=jnp.int32) - flat_hot
    slot_rank = jnp.sum(before * flat_hot, axis=1, dtype=jnp.int32).reshape(tok_rows, TOP)
    half = capacity // 2
    rows_in = jnp.concatenate([mixed_in, slot_cot])
    w_up_one = w_up[0]
    w_down_one = w_down[0]
    spots = jnp.arange(n_experts * 2 * half, dtype=jnp.int32)
    gathered = []
    grad_ups = []
    grad_downs = []
    for chunk in range(2):
        mine = slot_rank // half == chunk
        in_spot = jnp.where(mine, routes * (2 * half) + slot_rank % half, -1)
        cot_spot = jnp.where(mine, in_spot + half, -1)
        pick = jnp.concatenate(
            [
                (spots[:, None] == in_spot[None, :, 0]) | (spots[:, None] == in_spot[None, :, 1]),
                spots[:, None] == cot_spot.T.reshape(1, -1),
            ],
            axis=1,
        ).astype(jnp.bfloat16)
        sent = jnp.dot(pick, rows_in, preferred_element_type=jnp.float32).astype(jnp.bfloat16)
        recv = lax.all_to_all(
            sent.reshape(n_experts, 2 * half, feature_width), "expert", split_axis=0, concat_axis=0, tiled=True
        )
        flat_in = recv[:, :half].reshape(-1, feature_width)
        flat_cot = recv[:, half:].reshape(-1, feature_width)
        hidden, gelu_slope, outputs = expert_forward(flat_in, w_up_one, w_down_one)
        d_inputs, grad_up_part, grad_down_part = expert_backward(
            flat_in, flat_cot, hidden, gelu_slope, w_up_one, w_down_one
        )
        grad_ups.append(grad_up_part)
        grad_downs.append(grad_down_part)
        back = jnp.concatenate(
            [outputs.reshape(n_experts, half, feature_width), d_inputs.reshape(n_experts, half, feature_width)],
            axis=1,
        )
        back = lax.all_to_all(back, "expert", split_axis=0, concat_axis=0, tiled=True)
        take = jnp.concatenate(
            [
                in_spot.T.reshape(-1, 1) == spots[None, :],
                (cot_spot[:, 0:1] == spots[None, :]) | (cot_spot[:, 1:2] == spots[None, :]),
            ]
        ).astype(jnp.bfloat16)
        gathered.append(
            jnp.dot(take, back.reshape(-1, feature_width), preferred_element_type=jnp.float32)
        )
    sum_up = lax.psum((grad_ups[0] + grad_ups[1]).astype(jnp.bfloat16), "dp")
    sum_down = lax.psum((grad_downs[0] + grad_downs[1]).astype(jnp.bfloat16), "dp")
    picked = gathered[0] + gathered[1]
    expert_wide = jnp.stack([picked[k * tok_rows:(k + 1) * tok_rows] for k in range(TOP)], axis=1)
    grad_sum = picked[TOP * tok_rows:]
    layer_out = (
        mixed_in.astype(jnp.float32) + jnp.sum(gates[:, :, None] * expert_wide, axis=1)
    ).astype(jnp.bfloat16)
    d_gates = jnp.sum(expert_wide * cot_wide[:, None, :], axis=2)
    mean_term = jnp.sum(gates * d_gates, axis=1, keepdims=True)
    d_chosen = (d_gates - mean_term) / gate_total * squashed * (1.0 - squashed)
    d_logits = jnp.sum(jnp.where(route_hot, d_chosen[:, :, None], 0.0), axis=1)
    d_router = lax.dot_general(
        d_logits,
        router.astype(jnp.float32),
        (((1,), (1,)), ((), ())),
        precision=lax.Precision.HIGHEST,
    )
    grad_in = (cot_wide + grad_sum + d_router).astype(jnp.bfloat16)
    return (
        layer_out,
        grad_in,
        sum_up.astype(jnp.bfloat16)[None],
        sum_down.astype(jnp.bfloat16)[None],
    )


def solution(mesh):
    return jax.shard_map(
        per_device,
        mesh=mesh,
        in_specs=(
            P(("dp", "expert"), None),
            P(("dp", "expert")),
            P(("dp", "expert"), None),
            P(("dp", "expert"), None),
            P(),
            P(),
            P(),
            P(),
            P("expert", None, None),
            P("expert", None, None),
        ),
        out_specs=(
            P(("dp", "expert"), None),
            P(("dp", "expert"), None),
            P("expert", None, None),
            P("expert", None, None),
        ),
        check_vma=False,
    )
```

```python
import jax
import jax.numpy as jnp
from jax import lax
from jax.sharding import PartitionSpec as P

TOP = 2


coef_a = 0.7978845608028654
coef_b = 0.044715


def gelu_pair(pre_act):
    inner = coef_a * (pre_act + coef_b * pre_act * pre_act * pre_act)
    tanh_val = jnp.tanh(inner)
    activated = 0.5 * pre_act * (1.0 + tanh_val)
    gelu_slope = 0.5 * (1.0 + tanh_val) + 0.5 * pre_act * (1.0 - tanh_val * tanh_val) * coef_a * (
        1.0 + 3.0 * coef_b * pre_act * pre_act
    )
    return (activated, gelu_slope)


def contract_rows(left, right):
    return lax.dot_general(
        left, right, (((0,), (0,)), ((), ())), preferred_element_type=jnp.float32
    )


def contract_cols(left, right):
    return lax.dot_general(
        left, right, (((1,), (1,)), ((), ())), preferred_element_type=jnp.float32
    )


def expert_forward(flat_in, w_up_one, w_down_one):
    pre_act = jnp.dot(flat_in, w_up_one, preferred_element_type=jnp.float32)
    activated, gelu_slope = gelu_pair(pre_act)
    hidden = activated.astype(jnp.bfloat16)
    outputs = jnp.dot(hidden, w_down_one, preferred_element_type=jnp.float32).astype(jnp.bfloat16)
    return (hidden, gelu_slope, outputs)


def expert_backward(flat_in, flat_cot, hidden, gelu_slope, w_up_one, w_down_one):
    grad_down_part = contract_rows(hidden, flat_cot)
    d_hidden = contract_cols(flat_cot, w_down_one)
    d_pre = (d_hidden * gelu_slope).astype(jnp.bfloat16)
    d_inputs = contract_cols(d_pre, w_up_one).astype(jnp.bfloat16)
    grad_up_part = contract_rows(flat_in, d_pre)
    return (d_inputs, grad_up_part, grad_down_part)


def layer_body(
    features, slots, routes, cotangent, pos_table, tower_in, tower_out, router, w_up, w_down
):
    tok_rows = features.shape[0]
    feature_width = features.shape[1]
    n_experts = router.shape[1]
    capacity = 2 * TOP * tok_rows // n_experts
    pos_hidden = jax.nn.relu(jnp.dot(pos_table, tower_in, preferred_element_type=jnp.float32))
    pos_rows = jnp.dot(pos_hidden, tower_out.astype(jnp.float32), precision=lax.Precision.HIGHEST)
    slot_hot = (slots[:, None] == jnp.arange(pos_table.shape[0], dtype=jnp.int32)[None, :]).astype(
        jnp.float32
    )
    pos_feats = jnp.dot(slot_hot, pos_rows, precision=lax.Precision.HIGHEST)
    mixed_in = (features.astype(jnp.float32) + pos_feats).astype(jnp.bfloat16)
    logits = jnp.dot(mixed_in, router, preferred_element_type=jnp.float32)
    expert_ids = jnp.arange(n_experts, dtype=jnp.int32)
    route_hot = routes[:, :, None] == expert_ids[None, None, :]
    chosen = jnp.sum(jnp.where(route_hot, logits[:, None, :], 0.0), axis=2)
    squashed = 1.0 / (1.0 + jnp.exp(-chosen))
    gate_total = jnp.sum(squashed, axis=1, keepdims=True)
    gates = squashed / gate_total
    cot_wide = cotangent.astype(jnp.float32)
    slot_cot = jnp.concatenate(
        [(gates[:, k:k + 1] * cot_wide).astype(jnp.bfloat16) for k in range(TOP)]
    )
    flat_hot = route_hot.reshape(-1, n_experts).astype(jnp.int32)
    before = jnp.cumsum(flat_hot, axis=0, dtype=jnp.int32) - flat_hot
    slot_rank = jnp.sum(before * flat_hot, axis=1, dtype=jnp.int32).reshape(tok_rows, TOP)
    half = capacity // 2
    rows_in = jnp.concatenate([mixed_in, slot_cot])
    w_up_one = w_up[0]
    w_down_one = w_down[0]
    spots = jnp.arange(n_experts * 2 * half, dtype=jnp.int32)
    gathered = []
    backs = []
    spots_of = []
    grad_ups = []
    grad_downs = []
    for chunk in range(2):
        mine = slot_rank // half == chunk
        in_spot = jnp.where(mine, routes * (2 * half) + slot_rank % half, -1)
        cot_spot = jnp.where(mine, in_spot + half, -1)
        spots_of.append((in_spot, cot_spot))
        pick = jnp.concatenate(
            [
                (spots[:, None] == in_spot[None, :, 0]) | (spots[:, None] == in_spot[None, :, 1]),
                spots[:, None] == cot_spot.T.reshape(1, -1),
            ],
            axis=1,
        ).astype(jnp.bfloat16)
        sent = jnp.dot(pick, rows_in, preferred_element_type=jnp.float32).astype(jnp.bfloat16)
        recv = lax.all_to_all(
            sent.reshape(n_experts, 2 * half, feature_width), "expert", split_axis=0, concat_axis=0, tiled=True
        )
        flat_in = recv[:, :half].reshape(-1, feature_width)
        flat_cot = recv[:, half:].reshape(-1, feature_width)
        hidden, gelu_slope, outputs = expert_forward(flat_in, w_up_one, w_down_one)
        d_inputs, grad_up_part, grad_down_part = expert_backward(
            flat_in, flat_cot, hidden, gelu_slope, w_up_one, w_down_one
        )
        grad_ups.append(grad_up_part)
        grad_downs.append(grad_down_part)
        back = jnp.concatenate(
            [outputs.reshape(n_experts, half, feature_width), d_inputs.reshape(n_experts, half, feature_width)],
            axis=1,
        )
        backs.append(back)
    part_up = (grad_ups[0] + grad_ups[1]).astype(jnp.bfloat16)[None]
    part_down = (grad_downs[0] + grad_downs[1]).astype(jnp.bfloat16)[None]
    first_back, part_up, part_down = lax.optimization_barrier((backs[0], part_up, part_down))
    sum_up = lax.psum(part_up, "dp")
    sum_down = lax.psum(part_down, "dp")
    backs[0] = first_back
    for chunk in range(2):
        in_spot, cot_spot = spots_of[chunk]
        back = lax.all_to_all(backs[chunk], "expert", split_axis=0, concat_axis=0, tiled=True)
        take = jnp.concatenate(
            [
                in_spot.T.reshape(-1, 1) == spots[None, :],
                (cot_spot[:, 0:1] == spots[None, :]) | (cot_spot[:, 1:2] == spots[None, :]),
            ]
        ).astype(jnp.bfloat16)
        gathered.append(
            jnp.dot(take, back.reshape(-1, feature_width), preferred_element_type=jnp.float32)
        )
    picked = gathered[0] + gathered[1]
    expert_wide = jnp.stack([picked[k * tok_rows:(k + 1) * tok_rows] for k in range(TOP)], axis=1)
    grad_sum = picked[TOP * tok_rows:]
    layer_out = (
        mixed_in.astype(jnp.float32) + jnp.sum(gates[:, :, None] * expert_wide, axis=1)
    ).astype(jnp.bfloat16)
    d_gates = jnp.sum(expert_wide * cot_wide[:, None, :], axis=2)
    mean_term = jnp.sum(gates * d_gates, axis=1, keepdims=True)
    d_chosen = (d_gates - mean_term) / gate_total * squashed * (1.0 - squashed)
    d_logits = jnp.sum(jnp.where(route_hot, d_chosen[:, :, None], 0.0), axis=1)
    d_router = lax.dot_general(
        d_logits,
        router.astype(jnp.float32),
        (((1,), (1,)), ((), ())),
        precision=lax.Precision.HIGHEST,
    )
    grad_in = (cot_wide + grad_sum + d_router).astype(jnp.bfloat16)
    return (
        layer_out,
        grad_in,
        sum_up,
        sum_down,
    )


def solution(mesh):
    return shard_map_of(mesh)


def shard_map_of(mesh):
    return jax.shard_map(
        layer_body,
        mesh=mesh,
        in_specs=(
            P(("dp", "expert"), None),
            P(("dp", "expert")),
            P(("dp", "expert"), None),
            P(("dp", "expert"), None),
            P(),
            P(),
            P(),
            P(),
            P("expert", None, None),
            P("expert", None, None),
        ),
        out_specs=(
            P(("dp", "expert"), None),
            P(("dp", "expert"), None),
            P("expert", None, None),
            P("expert", None, None),
        ),
        check_vma=False,
    )
```

```python
import jax
import jax.numpy as jnp
from jax import lax
from jax.sharding import PartitionSpec as P

TOP = 2


coef_a = 0.7978845608028654
coef_b = 0.044715


def gelu_pair(pre_act):
    inner = coef_a * (pre_act + coef_b * pre_act * pre_act * pre_act)
    tanh_val = jnp.tanh(inner)
    activated = 0.5 * pre_act * (1.0 + tanh_val)
    gelu_slope = 0.5 * (1.0 + tanh_val) + 0.5 * pre_act * (1.0 - tanh_val * tanh_val) * coef_a * (
        1.0 + 3.0 * coef_b * pre_act * pre_act
    )
    return (activated, gelu_slope)


def contract_rows(left, right):
    return lax.dot_general(
        left, right, (((0,), (0,)), ((), ())), preferred_element_type=jnp.float32
    )


def contract_cols(left, right):
    return lax.dot_general(
        left, right, (((1,), (1,)), ((), ())), preferred_element_type=jnp.float32
    )


def expert_forward(flat_in, w_up_one, w_down_one):
    pre_act = jnp.dot(flat_in, w_up_one, preferred_element_type=jnp.float32)
    activated, gelu_slope = gelu_pair(pre_act)
    hidden = activated.astype(jnp.bfloat16)
    outputs = jnp.dot(hidden, w_down_one, preferred_element_type=jnp.float32).astype(jnp.bfloat16)
    return (hidden, gelu_slope, outputs)


def expert_backward(flat_in, flat_cot, hidden, gelu_slope, w_up_one, w_down_one):
    grad_down_part = contract_rows(hidden, flat_cot)
    d_hidden = contract_cols(flat_cot, w_down_one)
    d_pre = (d_hidden * gelu_slope).astype(jnp.bfloat16)
    d_inputs = contract_cols(d_pre, w_up_one).astype(jnp.bfloat16)
    grad_up_part = contract_rows(flat_in, d_pre)
    return (d_inputs, grad_up_part, grad_down_part)


def layer_body(
    features, slots, routes, cotangent, pos_table, tower_in, tower_out, router, w_up, w_down
):
    tok_rows = features.shape[0]
    feature_width = features.shape[1]
    n_experts = router.shape[1]
    capacity = 2 * TOP * tok_rows // n_experts
    pos_hidden = jax.nn.relu(jnp.dot(pos_table, tower_in, preferred_element_type=jnp.float32))
    pos_rows = jnp.dot(pos_hidden, tower_out.astype(jnp.float32), precision=lax.Precision.HIGHEST)
    slot_hot = (slots[:, None] == jnp.arange(pos_table.shape[0], dtype=jnp.int32)[None, :]).astype(
        jnp.float32
    )
    pos_feats = jnp.dot(slot_hot, pos_rows, precision=lax.Precision.HIGHEST)
    mixed_in = (features.astype(jnp.float32) + pos_feats).astype(jnp.bfloat16)
    logits = jnp.dot(mixed_in, router, preferred_element_type=jnp.float32)
    expert_ids = jnp.arange(n_experts, dtype=jnp.int32)
    route_hot = routes[:, :, None] == expert_ids[None, None, :]
    chosen = jnp.sum(jnp.where(route_hot, logits[:, None, :], 0.0), axis=2)
    squashed = 1.0 / (1.0 + jnp.exp(-chosen))
    gate_total = jnp.sum(squashed, axis=1, keepdims=True)
    gates = squashed / gate_total
    cot_wide = cotangent.astype(jnp.float32)
    slot_cot = jnp.concatenate(
        [(gates[:, k:k + 1] * cot_wide).astype(jnp.bfloat16) for k in range(TOP)]
    )
    flat_hot = jnp.concatenate([routes[:, k:k + 1] == expert_ids[None, :] for k in range(TOP)])
    order = jnp.arange(TOP * tok_rows, dtype=jnp.int32)
    earlier = (order[None, :] < order[:, None]).astype(jnp.bfloat16)
    before = jnp.dot(earlier, flat_hot.astype(jnp.bfloat16), preferred_element_type=jnp.float32)
    slot_rank = jnp.sum(jnp.where(flat_hot, before, 0.0), axis=1).astype(jnp.int32)
    slot_rank = slot_rank.reshape(TOP, tok_rows).T
    first_size = (5 * capacity) // 8
    bounds = ((0, first_size), (first_size, capacity - first_size))
    rows_in = jnp.concatenate([mixed_in, slot_cot])
    w_up_one = w_up[0]
    w_down_one = w_down[0]
    gathered = []
    backs = []
    spots_of = []
    grad_ups = []
    grad_downs = []
    for chunk in range(2):
        low, half = bounds[chunk]
        spots = jnp.arange(n_experts * 2 * half, dtype=jnp.int32)
        mine = (slot_rank >= low) & (slot_rank < low + half)
        in_spot = jnp.where(mine, routes * (2 * half) + slot_rank - low, -1)
        cot_spot = jnp.where(mine, in_spot + half, -1)
        spots_of.append((in_spot, cot_spot, spots))
        pick = jnp.concatenate(
            [
                (spots[:, None] == in_spot[None, :, 0]) | (spots[:, None] == in_spot[None, :, 1]),
                spots[:, None] == cot_spot.T.reshape(1, -1),
            ],
            axis=1,
        ).astype(jnp.bfloat16)
        sent = jnp.dot(pick, rows_in, preferred_element_type=jnp.float32).astype(jnp.bfloat16)
        recv = lax.all_to_all(
            sent.reshape(n_experts, 2 * half, feature_width), "expert", split_axis=0, concat_axis=0, tiled=True
        )
        flat_in = recv[:, :half].reshape(-1, feature_width)
        flat_cot = recv[:, half:].reshape(-1, feature_width)
        hidden, gelu_slope, outputs = expert_forward(flat_in, w_up_one, w_down_one)
        d_inputs, grad_up_part, grad_down_part = expert_backward(
            flat_in, flat_cot, hidden, gelu_slope, w_up_one, w_down_one
        )
        grad_ups.append(grad_up_part)
        grad_downs.append(grad_down_part)
        back = jnp.concatenate(
            [outputs.reshape(n_experts, half, feature_width), d_inputs.reshape(n_experts, half, feature_width)],
            axis=1,
        )
        backs.append(back)
    part_up = (grad_ups[0] + grad_ups[1]).astype(jnp.bfloat16)[None]
    part_down = (grad_downs[0] + grad_downs[1]).astype(jnp.bfloat16)[None]
    first_back, part_up, part_down = lax.optimization_barrier((backs[0], part_up, part_down))
    sum_up = lax.psum(part_up, "dp")
    sum_down = lax.psum(part_down, "dp")
    backs[0] = first_back
    for chunk in range(2):
        in_spot, cot_spot, spots = spots_of[chunk]
        back = lax.all_to_all(backs[chunk], "expert", split_axis=0, concat_axis=0, tiled=True)
        take = jnp.concatenate(
            [
                in_spot.T.reshape(-1, 1) == spots[None, :],
                (cot_spot[:, 0:1] == spots[None, :]) | (cot_spot[:, 1:2] == spots[None, :]),
            ]
        ).astype(jnp.bfloat16)
        gathered.append(
            jnp.dot(take, back.reshape(-1, feature_width), preferred_element_type=jnp.float32)
        )
    picked = gathered[0] + gathered[1]
    expert_wide = jnp.stack([picked[k * tok_rows:(k + 1) * tok_rows] for k in range(TOP)], axis=1)
    grad_sum = picked[TOP * tok_rows:]
    layer_out = (
        mixed_in.astype(jnp.float32) + jnp.sum(gates[:, :, None] * expert_wide, axis=1)
    ).astype(jnp.bfloat16)
    d_gates = jnp.sum(expert_wide * cot_wide[:, None, :], axis=2)
    mean_term = jnp.sum(gates * d_gates, axis=1, keepdims=True)
    d_chosen = (d_gates - mean_term) / gate_total * squashed * (1.0 - squashed)
    d_logits = jnp.sum(jnp.where(route_hot, d_chosen[:, :, None], 0.0), axis=1)
    d_router = lax.dot_general(
        d_logits,
        router.astype(jnp.float32),
        (((1,), (1,)), ((), ())),
        precision=lax.Precision.HIGHEST,
    )
    grad_in = (cot_wide + grad_sum + d_router).astype(jnp.bfloat16)
    return (
        layer_out,
        grad_in,
        sum_up,
        sum_down,
    )


def solution(mesh):
    return shard_map_of(mesh)


def shard_map_of(mesh):
    return jax.shard_map(
        layer_body,
        mesh=mesh,
        in_specs=(
            P(("dp", "expert"), None),
            P(("dp", "expert")),
            P(("dp", "expert"), None),
            P(("dp", "expert"), None),
            P(),
            P(),
            P(),
            P(),
            P("expert", None, None),
            P("expert", None, None),
        ),
        out_specs=(
            P(("dp", "expert"), None),
            P(("dp", "expert"), None),
            P("expert", None, None),
            P("expert", None, None),
        ),
        check_vma=False,
    )
```

```python
import jax
import jax.numpy as jnp
from jax import lax
from jax.sharding import PartitionSpec as P

TOP = 2


coef_a = 0.7978845608028654
coef_b = 0.044715


def gelu_pair(pre_act):
    inner = coef_a * (pre_act + coef_b * pre_act * pre_act * pre_act)
    tanh_val = jnp.tanh(inner)
    activated = 0.5 * pre_act * (1.0 + tanh_val)
    gelu_slope = 0.5 * (1.0 + tanh_val) + 0.5 * pre_act * (1.0 - tanh_val * tanh_val) * coef_a * (
        1.0 + 3.0 * coef_b * pre_act * pre_act
    )
    return (activated, gelu_slope)


def contract_rows(left, right):
    return lax.dot_general(
        left, right, (((0,), (0,)), ((), ())), preferred_element_type=jnp.float32
    )


def contract_cols(left, right):
    return lax.dot_general(
        left, right, (((1,), (1,)), ((), ())), preferred_element_type=jnp.float32
    )


def expert_forward(flat_in, w_up_one, w_down_one):
    pre_act = jnp.dot(flat_in, w_up_one, preferred_element_type=jnp.float32)
    activated, gelu_slope = gelu_pair(pre_act)
    hidden, gelu_slope = lax.optimization_barrier((activated.astype(jnp.bfloat16), gelu_slope))
    outputs = jnp.dot(hidden, w_down_one, preferred_element_type=jnp.float32).astype(jnp.bfloat16)
    return (hidden, gelu_slope, outputs)


def expert_backward(flat_in, flat_cot, hidden, gelu_slope, w_up_one, w_down_one):
    grad_down_part = contract_rows(hidden, flat_cot)
    d_hidden = contract_cols(flat_cot, w_down_one)
    d_pre = (d_hidden * gelu_slope).astype(jnp.bfloat16)
    d_inputs = contract_cols(d_pre, w_up_one).astype(jnp.bfloat16)
    grad_up_part = contract_rows(flat_in, d_pre)
    return (d_inputs, grad_up_part, grad_down_part)


def layer_body(
    features, slots, routes, cotangent, pos_table, tower_in, tower_out, router, w_up, w_down
):
    tok_rows = features.shape[0]
    feature_width = features.shape[1]
    n_experts = router.shape[1]
    capacity = 2 * TOP * tok_rows // n_experts
    pos_hidden = jax.nn.relu(jnp.dot(pos_table, tower_in, preferred_element_type=jnp.float32))
    pos_rows = jnp.dot(pos_hidden, tower_out.astype(jnp.float32), precision=lax.Precision.HIGHEST)
    slot_hot = (slots[:, None] == jnp.arange(pos_table.shape[0], dtype=jnp.int32)[None, :]).astype(
        jnp.float32
    )
    pos_feats = jnp.dot(slot_hot, pos_rows, precision=lax.Precision.HIGHEST)
    mixed_in = (features.astype(jnp.float32) + pos_feats).astype(jnp.bfloat16)
    logits = jnp.dot(mixed_in, router, preferred_element_type=jnp.float32)
    expert_ids = jnp.arange(n_experts, dtype=jnp.int32)
    route_hot = routes[:, :, None] == expert_ids[None, None, :]
    chosen = jnp.sum(jnp.where(route_hot, logits[:, None, :], 0.0), axis=2)
    squashed = 1.0 / (1.0 + jnp.exp(-chosen))
    gate_total = jnp.sum(squashed, axis=1, keepdims=True)
    gates = squashed / gate_total
    cot_wide = cotangent.astype(jnp.float32)
    slot_cot = jnp.concatenate(
        [(gates[:, k:k + 1] * cot_wide).astype(jnp.bfloat16) for k in range(TOP)]
    )
    flat_hot = jnp.concatenate([routes[:, k:k + 1] == expert_ids[None, :] for k in range(TOP)])
    order = jnp.arange(TOP * tok_rows, dtype=jnp.int32)
    earlier = (order[None, :] < order[:, None]).astype(jnp.bfloat16)
    before = jnp.dot(earlier, flat_hot.astype(jnp.bfloat16), preferred_element_type=jnp.float32)
    slot_rank = jnp.sum(jnp.where(flat_hot, before, 0.0), axis=1).astype(jnp.int32)
    slot_rank = slot_rank.reshape(TOP, tok_rows).T
    half = capacity // 2
    rows_in = jnp.concatenate([mixed_in, slot_cot])
    w_up_one = w_up[0]
    w_down_one = w_down[0]
    spots = jnp.arange(n_experts * 2 * half, dtype=jnp.int32)
    gathered = []
    backs = []
    spots_of = []
    grad_ups = []
    grad_downs = []
    for chunk in range(2):
        mine = slot_rank // half == chunk
        in_spot = jnp.where(mine, routes * (2 * half) + slot_rank % half, -1)
        cot_spot = jnp.where(mine, in_spot + half, -1)
        spots_of.append((in_spot, cot_spot))
        pick = jnp.concatenate(
            [
                (spots[:, None] == in_spot[None, :, 0]) | (spots[:, None] == in_spot[None, :, 1]),
                spots[:, None] == cot_spot.T.reshape(1, -1),
            ],
            axis=1,
        ).astype(jnp.bfloat16)
        sent = jnp.dot(pick, rows_in, preferred_element_type=jnp.float32).astype(jnp.bfloat16)
        recv = lax.all_to_all(
            sent.reshape(n_experts, 2 * half, feature_width), "expert", split_axis=0, concat_axis=0, tiled=True
        )
        flat_in = recv[:, :half].reshape(-1, feature_width)
        flat_cot = recv[:, half:].reshape(-1, feature_width)
        hidden, gelu_slope, outputs = expert_forward(flat_in, w_up_one, w_down_one)
        d_inputs, grad_up_part, grad_down_part = expert_backward(
            flat_in, flat_cot, hidden, gelu_slope, w_up_one, w_down_one
        )
        grad_ups.append(grad_up_part)
        grad_downs.append(grad_down_part)
        back = jnp.concatenate(
            [outputs.reshape(n_experts, half, feature_width), d_inputs.reshape(n_experts, half, feature_width)],
            axis=1,
        )
        backs.append(back)
    part_up = (grad_ups[0] + grad_ups[1]).astype(jnp.bfloat16)[None]
    part_down = (grad_downs[0] + grad_downs[1]).astype(jnp.bfloat16)[None]
    first_back, part_up, part_down = lax.optimization_barrier((backs[0], part_up, part_down))
    sum_up = lax.psum(part_up, "dp")
    sum_down = lax.psum(part_down, "dp")
    backs[0] = first_back
    for chunk in range(2):
        in_spot, cot_spot = spots_of[chunk]
        back = lax.all_to_all(backs[chunk], "expert", split_axis=0, concat_axis=0, tiled=True)
        take = jnp.concatenate(
            [
                in_spot.T.reshape(-1, 1) == spots[None, :],
                (cot_spot[:, 0:1] == spots[None, :]) | (cot_spot[:, 1:2] == spots[None, :]),
            ]
        ).astype(jnp.bfloat16)
        gathered.append(
            jnp.dot(take, back.reshape(-1, feature_width), preferred_element_type=jnp.float32)
        )
    picked = gathered[0] + gathered[1]
    expert_wide = jnp.stack([picked[k * tok_rows:(k + 1) * tok_rows] for k in range(TOP)], axis=1)
    grad_sum = picked[TOP * tok_rows:]
    layer_out = (
        mixed_in.astype(jnp.float32) + jnp.sum(gates[:, :, None] * expert_wide, axis=1)
    ).astype(jnp.bfloat16)
    d_gates = jnp.sum(expert_wide * cot_wide[:, None, :], axis=2)
    mean_term = jnp.sum(gates * d_gates, axis=1, keepdims=True)
    d_chosen = (d_gates - mean_term) / gate_total * squashed * (1.0 - squashed)
    d_logits = jnp.sum(jnp.where(route_hot, d_chosen[:, :, None], 0.0), axis=1)
    d_router = lax.dot_general(
        d_logits,
        router.astype(jnp.float32),
        (((1,), (1,)), ((), ())),
        precision=lax.Precision.HIGHEST,
    )
    grad_in = (cot_wide + grad_sum + d_router).astype(jnp.bfloat16)
    return (
        layer_out,
        grad_in,
        sum_up,
        sum_down,
    )


def solution(mesh):
    return shard_map_of(mesh)


def shard_map_of(mesh):
    return jax.shard_map(
        layer_body,
        mesh=mesh,
        in_specs=(
            P(("dp", "expert"), None),
            P(("dp", "expert")),
            P(("dp", "expert"), None),
            P(("dp", "expert"), None),
            P(),
            P(),
            P(),
            P(),
            P("expert", None, None),
            P("expert", None, None),
        ),
        out_specs=(
            P(("dp", "expert"), None),
            P(("dp", "expert"), None),
            P("expert", None, None),
            P("expert", None, None),
        ),
        check_vma=False,
    )
```

```python
import jax
import jax.numpy as jnp
from jax import lax
from jax.sharding import PartitionSpec as P

TOP = 2


coef_a = 0.7978845608028654
coef_b = 0.044715


def gelu_pair(pre_act):
    inner = coef_a * (pre_act + coef_b * pre_act * pre_act * pre_act)
    tanh_val = jnp.tanh(inner)
    activated = 0.5 * pre_act * (1.0 + tanh_val)
    gelu_slope = 0.5 * (1.0 + tanh_val) + 0.5 * pre_act * (1.0 - tanh_val * tanh_val) * coef_a * (
        1.0 + 3.0 * coef_b * pre_act * pre_act
    )
    return (activated, gelu_slope)


def contract_rows(left, right):
    return lax.dot_general(
        left, right, (((0,), (0,)), ((), ())), preferred_element_type=jnp.float32
    )


def contract_cols(left, right):
    return lax.dot_general(
        left, right, (((1,), (1,)), ((), ())), preferred_element_type=jnp.float32
    )


def expert_forward(flat_in, w_up_one, w_down_one):
    pre_act = jnp.dot(flat_in, w_up_one, preferred_element_type=jnp.float32)
    activated, gelu_slope = gelu_pair(pre_act)
    hidden = activated.astype(jnp.bfloat16)
    outputs = jnp.dot(hidden, w_down_one, preferred_element_type=jnp.float32).astype(jnp.bfloat16)
    return (hidden, gelu_slope, outputs)


def expert_backward(flat_in, flat_cot, hidden, gelu_slope, w_up_one, w_down_one):
    grad_down_part = contract_rows(hidden, flat_cot)
    d_hidden = contract_cols(flat_cot, w_down_one)
    d_pre = (d_hidden * gelu_slope).astype(jnp.bfloat16)
    d_inputs = contract_cols(d_pre, w_up_one).astype(jnp.bfloat16)
    grad_up_part = contract_rows(flat_in, d_pre)
    return (d_inputs, grad_up_part, grad_down_part)


def layer_body(
    features, slots, routes, cotangent, pos_table, tower_in, tower_out, router, w_up, w_down
):
    tok_rows = features.shape[0]
    feature_width = features.shape[1]
    n_experts = router.shape[1]
    capacity = 2 * TOP * tok_rows // n_experts
    pos_hidden = jax.nn.relu(jnp.dot(pos_table, tower_in, preferred_element_type=jnp.float32))
    pos_rows = jnp.dot(pos_hidden, tower_out.astype(jnp.float32), precision=lax.Precision.HIGHEST)
    pos_feats = jnp.take(pos_rows, slots, axis=0)
    mixed_in = (features.astype(jnp.float32) + pos_feats).astype(jnp.bfloat16)
    logits = jnp.dot(mixed_in, router, preferred_element_type=jnp.float32)
    expert_ids = jnp.arange(n_experts, dtype=jnp.int32)
    route_hot = routes[:, :, None] == expert_ids[None, None, :]
    chosen = jnp.sum(jnp.where(route_hot, logits[:, None, :], 0.0), axis=2)
    squashed = 1.0 / (1.0 + jnp.exp(-chosen))
    gate_total = jnp.sum(squashed, axis=1, keepdims=True)
    gates = squashed / gate_total
    cot_wide = cotangent.astype(jnp.float32)
    slot_cot = jnp.concatenate(
        [(gates[:, k:k + 1] * cot_wide).astype(jnp.bfloat16) for k in range(TOP)]
    )
    flat_hot = jnp.concatenate([routes[:, k:k + 1] == expert_ids[None, :] for k in range(TOP)])
    order = jnp.arange(TOP * tok_rows, dtype=jnp.int32)
    earlier = (order[None, :] < order[:, None]).astype(jnp.bfloat16)
    before = jnp.dot(earlier, flat_hot.astype(jnp.bfloat16), preferred_element_type=jnp.float32)
    slot_rank = jnp.sum(jnp.where(flat_hot, before, 0.0), axis=1).astype(jnp.int32)
    slot_rank = slot_rank.reshape(TOP, tok_rows).T
    half = capacity // 2
    rows_in = jnp.concatenate([mixed_in, slot_cot])
    w_up_one = w_up[0]
    w_down_one = w_down[0]
    spots = jnp.arange(n_experts * 2 * half, dtype=jnp.int32)
    gathered = []
    backs = []
    spots_of = []
    grad_ups = []
    grad_downs = []
    for chunk in range(2):
        mine = slot_rank // half == chunk
        in_spot = jnp.where(mine, routes * (2 * half) + slot_rank % half, -1)
        cot_spot = jnp.where(mine, in_spot + half, -1)
        spots_of.append((in_spot, cot_spot))
        pick = jnp.concatenate(
            [
                (spots[:, None] == in_spot[None, :, 0]) | (spots[:, None] == in_spot[None, :, 1]),
                spots[:, None] == cot_spot.T.reshape(1, -1),
            ],
            axis=1,
        ).astype(jnp.bfloat16)
        sent = jnp.dot(pick, rows_in, preferred_element_type=jnp.float32).astype(jnp.bfloat16)
        recv = lax.all_to_all(
            sent.reshape(n_experts, 2 * half, feature_width), "expert", split_axis=0, concat_axis=0, tiled=True
        )
        flat_in = recv[:, :half].reshape(-1, feature_width)
        flat_cot = recv[:, half:].reshape(-1, feature_width)
        hidden, gelu_slope, outputs = expert_forward(flat_in, w_up_one, w_down_one)
        d_inputs, grad_up_part, grad_down_part = expert_backward(
            flat_in, flat_cot, hidden, gelu_slope, w_up_one, w_down_one
        )
        grad_ups.append(grad_up_part)
        grad_downs.append(grad_down_part)
        back = jnp.concatenate(
            [outputs.reshape(n_experts, half, feature_width), d_inputs.reshape(n_experts, half, feature_width)],
            axis=1,
        )
        backs.append(back)
    part_up = (grad_ups[0] + grad_ups[1]).astype(jnp.bfloat16)[None]
    part_down = (grad_downs[0] + grad_downs[1]).astype(jnp.bfloat16)[None]
    first_back, part_up, part_down = lax.optimization_barrier((backs[0], part_up, part_down))
    sum_up = lax.psum(part_up, "dp")
    sum_down = lax.psum(part_down, "dp")
    backs[0] = first_back
    for chunk in range(2):
        in_spot, cot_spot = spots_of[chunk]
        back = lax.all_to_all(backs[chunk], "expert", split_axis=0, concat_axis=0, tiled=True)
        take = jnp.concatenate(
            [
                in_spot.T.reshape(-1, 1) == spots[None, :],
                (cot_spot[:, 0:1] == spots[None, :]) | (cot_spot[:, 1:2] == spots[None, :]),
            ]
        ).astype(jnp.bfloat16)
        gathered.append(
            jnp.dot(take, back.reshape(-1, feature_width), preferred_element_type=jnp.float32)
        )
    picked = gathered[0] + gathered[1]
    expert_wide = jnp.stack([picked[k * tok_rows:(k + 1) * tok_rows] for k in range(TOP)], axis=1)
    grad_sum = picked[TOP * tok_rows:]
    layer_out = (
        mixed_in.astype(jnp.float32) + jnp.sum(gates[:, :, None] * expert_wide, axis=1)
    ).astype(jnp.bfloat16)
    d_gates = jnp.sum(expert_wide * cot_wide[:, None, :], axis=2)
    mean_term = jnp.sum(gates * d_gates, axis=1, keepdims=True)
    d_chosen = (d_gates - mean_term) / gate_total * squashed * (1.0 - squashed)
    d_logits = jnp.sum(jnp.where(route_hot, d_chosen[:, :, None], 0.0), axis=1)
    d_router = lax.dot_general(
        d_logits,
        router.astype(jnp.float32),
        (((1,), (1,)), ((), ())),
        precision=lax.Precision.HIGHEST,
    )
    grad_in = (cot_wide + grad_sum + d_router).astype(jnp.bfloat16)
    return (
        layer_out,
        grad_in,
        sum_up,
        sum_down,
    )


def solution(mesh):
    return shard_map_of(mesh)


def shard_map_of(mesh):
    return jax.shard_map(
        layer_body,
        mesh=mesh,
        in_specs=(
            P(("dp", "expert"), None),
            P(("dp", "expert")),
            P(("dp", "expert"), None),
            P(("dp", "expert"), None),
            P(),
            P(),
            P(),
            P(),
            P("expert", None, None),
            P("expert", None, None),
        ),
        out_specs=(
            P(("dp", "expert"), None),
            P(("dp", "expert"), None),
            P("expert", None, None),
            P("expert", None, None),
        ),
        check_vma=False,
    )
```
